512 devices in a mesh: tiles: 128 (over y, z, core), days: 4 (over x).
Axes of the slice: x: 4, y: 8, z: 8, core: 2. Of those that a mesh axis runs over, the one named last changes fastest.
Arguments:
- observed: bfloat16 [32, 4096, 256], P('days', 'tiles'), may hold values from -4 to 4
- knot_base: bfloat16 [2048, 2, 512], P('tiles', None, 'days'), may hold values from -3 to -2
- knot_steps: bfloat16 [2048, 2, 99, 512], P('tiles', None, None, 'days'), may hold values from 0.019897461 to 0.08984375
- block_route: int32 [2048], P('tiles'), may hold values from 0 to 2047, as said below
- land_mask: int32 [4096, 256], P('tiles'), may hold values 0 or 1
- terrain: float32 [4096, 256], P('tiles'), may hold values from 0.5 to 2
Outputs:
- adjusted: float32 [32, 4096, 256], P('days', 'tiles')
The draws below stay inside these ranges and needn't reach their ends.
Inputs may be any that keep to these rules, and one draw needn't show every extreme that they name: block_route is a permutation of the blocks; the positions of one tiles device serve blocks of exactly 16 tile owners, 1 block of each.
All inputs are finite; a program needn't handle non-finite values. No bound on the sum of `land_mask` on one device may be relied on, other than what follows from the above.
Results may differ from the reference program's by a relative error of at most 0.005.
Values may be sent and summed in bfloat16 or wider, within the bound.
No kernel may reach another device: no remote copies, remote signals or barrier semaphores. Data moves between devices by JAX's collectives and lax.ppermute only.
A program may use at most 64 MiB of HBM per device.

```python
import math
import jax
import jax.numpy as jnp
from jax import lax

COLS = 256
KNOTS = 100
PASSES = 4
BLOCKS_DEV = 16
DAYS = 32
CAP = 1
NBLK = 2048
ROWS = 4096
CELLB = 512
N_TILES = 128


def draw_block_route(key, part):
    groups = BLOCKS_DEV // CAP
    key_off, key_src, key_dst, key_rel, key_rot = jax.random.split(key, 5)
    offsets = jax.random.permutation(key_off, N_TILES)[:groups]
    relabel = jax.random.permutation(key_rel, N_TILES)
    rotate = jax.random.permutation(key_rot, N_TILES)
    src_order = jax.vmap(lambda sub: jax.random.permutation(sub, BLOCKS_DEV))(jax.random.split(key_src, N_TILES))
    dst_order = jax.vmap(lambda sub: jax.random.permutation(sub, BLOCKS_DEV))(jax.random.split(key_dst, N_TILES))
    source = jnp.arange(N_TILES)[:, None]
    circle = (rotate[source] + offsets[src_order // CAP]) % N_TILES
    target = relabel[circle]
    place_slot = dst_order[target, src_order]
    return (target * BLOCKS_DEV + place_slot).reshape(-1).astype(jnp.int32)


def with_ends(entries, stream_key, low, largest):
    longest = entries.shape.index(max(entries.shape))
    spots = []
    for shift in (0, 1):
        where = [jax.random.randint(jax.random.fold_in(stream_key, axis), (), 0, length) for axis, length in enumerate(entries.shape)]
        where[longest] = (where[longest] + shift) % entries.shape[longest]
        spots.append(tuple(where))
    return entries.at[spots[0]].set(low).at[spots[1]].set(largest)


def steps_of(rng, shape, shards, least, high):
    def one(dim, blocks):
        heights = jax.random.uniform(jax.random.fold_in(jax.random.fold_in(rng, 6), dim), (blocks,), jnp.float32, least / len(shards), high / len(shards))
        return jnp.repeat(jnp.exp(heights), shape[dim] // blocks).reshape((-1,) + (1,) * (len(shape) - dim - 1))

    loudness = one(*shards[0])
    for cut in shards[1:]:
        loudness = loudness * one(*cut)
    return loudness


def centred(own_key, dims, width, most, cuts=(), kind=jnp.bfloat16):
    gain = steps_of(own_key, dims, cuts, -0.22, 0.18) if cuts else 1.0
    result = jax.random.normal(own_key, dims, jnp.float32) * width * gain
    return jnp.minimum(jnp.maximum(result, -most), most).astype(kind)


def setup_inputs(seed: int = 0) -> dict:
    splits = jax.random.split(jax.random.key(seed), 7)
    return {
        "observed": centred(splits[0], (DAYS, ROWS, COLS), 1.0, 4.0, ((0, 4), (1, 128))),
        "knot_base": jnp.clip(-3.0 + 1.0 * jax.random.uniform(splits[1], (NBLK, 2, CELLB), jnp.float32) ** steps_of(splits[1], (NBLK, 2, CELLB), ((0, 128), (2, 4)), -0.2, 0.2), -3.0, -2.0).astype(jnp.bfloat16),
        "knot_steps": jnp.clip(jnp.exp(math.log(0.08984375) - 1.5074799 * jax.random.uniform(splits[2], (NBLK, 2, KNOTS - 1, CELLB), jnp.float32) ** steps_of(splits[2], (NBLK, 2, KNOTS - 1, CELLB), ((0, 128), (3, 4)), -0.2, 0.2)), 0.019897461, 0.08984375).astype(jnp.bfloat16),
        "block_route": draw_block_route(jax.random.fold_in(splits[6], 71), 0),
        "land_mask": with_ends((jax.random.randint(splits[4], (ROWS, COLS), 0, 4) < 3).astype(jnp.int32), jax.random.fold_in(splits[4], 1), 0, 1),
        "terrain": jnp.clip(jnp.exp(math.log(2.0) - 1.3862944 * jax.random.uniform(splits[5], (ROWS, COLS), jnp.float32) ** steps_of(splits[5], (ROWS, COLS), ((0, 128),), -0.2, 0.2)), 0.5, 2.0),
    }


center_share = 0.5


def quantile_map(values, anchor, increments):
    step_x = increments[:, 0].astype(jnp.float32)
    step_y = increments[:, 1].astype(jnp.float32)
    position = anchor[:, 0][:, None, :].astype(jnp.float32) + jnp.cumsum(step_x, axis=1) - step_x
    slopes = step_y / step_x
    covered = jnp.clip(values.astype(jnp.float32)[:, :, None, :] - position[None], 0.0, step_x[None])
    return anchor[:, 1].astype(jnp.float32)[None] + jnp.sum(slopes[None] * covered, axis=2)


def neighbour_sum(padded):
    return padded[..., :-2, 1:-1] + padded[..., 2:, 1:-1] + padded[..., 1:-1, :-2] + padded[..., 1:-1, 2:]


def reference(observed, knot_base, knot_steps, block_route, land_mask, terrain):
    day_total, row_count, columns = observed.shape
    block_total = knot_base.shape[0]
    block_cells = 2 * columns
    group_size = 16
    groups = block_total // group_size
    tile_base = jnp.zeros_like(knot_base).at[block_route].set(knot_base)
    tile_steps = jnp.zeros_like(knot_steps).at[block_route].set(knot_steps)
    values = observed.reshape(day_total, groups, group_size, block_cells).transpose(1, 0, 2, 3)
    base_groups = tile_base.reshape(groups, group_size, 2, block_cells)
    step_groups = tile_steps.reshape(groups, group_size, 2, -1, block_cells)

    def one_group(group_args):
        return quantile_map(group_args[0], group_args[1], group_args[2]).astype(jnp.bfloat16)

    mapped = lax.map(one_group, (values, base_groups, step_groups))
    mapped = mapped.transpose(1, 0, 2, 3).reshape(day_total, row_count, columns)
    weights = terrain * land_mask.astype(jnp.float32)
    center = center_share * terrain
    denominator = center + neighbour_sum(jnp.pad(weights, 1))
    field = mapped.astype(jnp.float32)
    for sweep in range(PASSES):
        padded = jnp.pad(field * weights[None], ((0, 0), (1, 1), (1, 1)))
        field = (center[None] * field + neighbour_sum(padded)) / denominator[None]
    return field
```

```python
import jax
import jax.numpy as jnp
from jax import lax
from jax.sharding import PartitionSpec as P

PASSES = 4


center_share = 0.5


def neighbour_sum(padded):
    return (
        padded[..., :-2, 1:-1]
        + padded[..., 2:, 1:-1]
        + padded[..., 1:-1, :-2]
        + padded[..., 1:-1, 2:]
    )


def with_halo(cells, width):
    count = lax.axis_size("tiles")
    head = cells[..., :width, :]
    tail = cells[..., cells.shape[-2] - width :, :]
    from_above = lax.ppermute(tail, "tiles", [(i, i + 1) for i in range(count - 1)])
    from_below = lax.ppermute(head, "tiles", [(i + 1, i) for i in range(count - 1)])
    return jnp.concatenate([from_above, cells, from_below], axis=-2)


def quantile_map(values, anchor, increments):
    step_x = increments[:, 0].astype(jnp.float32)
    step_y = increments[:, 1].astype(jnp.float32)
    position = anchor[:, 0][:, None, :].astype(jnp.float32) + jnp.cumsum(step_x, axis=1) - step_x
    slopes = step_y / step_x
    covered = jnp.clip(
        values.astype(jnp.float32)[:, :, None, :] - position[:, None], 0.0, step_x[:, None]
    )
    total = jnp.sum(slopes[:, None] * covered, axis=2)
    return (anchor[:, 1].astype(jnp.float32)[:, None, :] + total).astype(jnp.bfloat16)


def body(observed, knot_base, knot_steps, block_route, land_mask, terrain):
    day_count, row_count, columns = observed.shape
    ntiles = lax.axis_size("tiles")
    ndays = lax.axis_size("days")
    owned = row_count // 2
    quarter = knot_base.shape[2]
    served = block_route.shape[0]
    tile_ids = jnp.arange(ntiles, dtype=jnp.int32)

    target = block_route // owned
    place_slot = block_route % owned
    match = target[None, :] == tile_ids[:, None]
    has = jnp.any(match, axis=1)
    slot_table = jnp.where(has, jnp.sum(jnp.where(match, place_slot[None, :], 0), axis=1), owned)
    local_of = jnp.sum(jnp.where(match, jnp.arange(served, dtype=jnp.int32)[None, :], 0), axis=1)

    recv_slot = lax.all_to_all(
        slot_table.reshape(ntiles, 1).astype(jnp.int32), "tiles", 0, 0, tiled=True
    ).reshape(ntiles)

    picked = jnp.minimum(recv_slot, owned - 1)
    holder = jnp.sum(
        jnp.where(
            recv_slot[None, :] == jnp.arange(owned, dtype=jnp.int32)[:, None], tile_ids[None, :], 0
        ),
        axis=1,
    )

    local = observed.reshape(day_count, owned, ndays, quarter)
    outgoing = jnp.take(local, picked, axis=1)
    outgoing = outgoing.transpose(1, 2, 0, 3).reshape(ntiles * ndays, day_count, quarter)
    arrived = lax.all_to_all(outgoing, ("tiles", "days"), 0, 0, tiled=True)
    arrived = arrived.reshape(ntiles, ndays * day_count, quarter)
    own_rows = jnp.take(arrived, target, axis=0)

    mapped_part = quantile_map(own_rows, knot_base, knot_steps)

    packed = jnp.take(mapped_part, local_of, axis=0)
    packed = packed.reshape(ntiles * ndays, day_count, quarter)
    returned = lax.all_to_all(packed, ("tiles", "days"), 0, 0, tiled=True)
    returned = returned.reshape(ntiles, ndays, day_count, quarter)
    blocks = jnp.take(returned, holder, axis=0)
    mapped = blocks.transpose(2, 0, 1, 3).reshape(day_count, row_count, columns)

    depth = PASSES
    weights = terrain * land_mask.astype(jnp.float32)
    wide_maps = with_halo(jnp.stack([weights, terrain]), depth)
    wide_weights = wide_maps[0]
    wide_center = center_share * wide_maps[1]
    wide_denom = wide_center + neighbour_sum(jnp.pad(wide_weights, 1))
    wide_denom = jnp.where(wide_denom > 0.0, wide_denom, 1.0)
    wide_field = with_halo(mapped, depth).astype(jnp.float32)
    for sweep in range(PASSES):
        padded = jnp.pad(wide_field * wide_weights[None], ((0, 0), (1, 1), (1, 1)))
        wide_field = (wide_center[None] * wide_field + neighbour_sum(padded)) / wide_denom[None]
    return wide_field[:, depth : depth + row_count, :]


def solution(mesh):
    return jax.shard_map(
        body,
        mesh=mesh,
        in_specs=(
            P("days", "tiles", None),
            P("tiles", None, "days"),
            P("tiles", None, None, "days"),
            P("tiles"),
            P("tiles", None),
            P("tiles", None),
        ),
        out_specs=P("days", "tiles", None),
        check_vma=False,
    )
```

```python
import jax
import jax.numpy as jnp
from jax import lax
from jax.sharding import PartitionSpec as P

PASSES = 4


center_share = 0.5


def neighbour_sum(padded):
    return (
        padded[..., :-2, 1:-1]
        + padded[..., 2:, 1:-1]
        + padded[..., 1:-1, :-2]
        + padded[..., 1:-1, 2:]
    )


def with_halo(cells, width):
    count = lax.axis_size("tiles")
    head = cells[..., :width, :]
    tail = cells[..., cells.shape[-2] - width :, :]
    from_above = lax.ppermute(tail, "tiles", [(i, i + 1) for i in range(count - 1)])
    from_below = lax.ppermute(head, "tiles", [(i + 1, i) for i in range(count - 1)])
    return jnp.concatenate([from_above, cells, from_below], axis=-2)


def quantile_map(values, anchor, increments):
    step_x = increments[:, 0].astype(jnp.float32)
    step_y = increments[:, 1].astype(jnp.float32)
    position = anchor[:, 0][:, None, :].astype(jnp.float32) + jnp.cumsum(step_x, axis=1) - step_x
    slopes = step_y / step_x
    covered = jnp.clip(
        values.astype(jnp.float32)[:, :, None, :] - position[:, None], 0.0, step_x[:, None]
    )
    total = jnp.sum(slopes[:, None] * covered, axis=2)
    return (anchor[:, 1].astype(jnp.float32)[:, None, :] + total).astype(jnp.bfloat16)


def body(observed, knot_base, knot_steps, block_route, land_mask, terrain):
    day_count, row_count, columns = observed.shape
    ntiles = lax.axis_size("tiles")
    ndays = lax.axis_size("days")
    owned = row_count // 2
    quarter = knot_base.shape[2]
    served = block_route.shape[0]
    tile_ids = jnp.arange(ntiles, dtype=jnp.int32)

    target = block_route // owned
    place_slot = block_route % owned
    match = target[None, :] == tile_ids[:, None]
    has = jnp.any(match, axis=1)
    slot_table = jnp.where(has, jnp.sum(jnp.where(match, place_slot[None, :], 0), axis=1), owned)
    local_of = jnp.sum(jnp.where(match, jnp.arange(served, dtype=jnp.int32)[None, :], 0), axis=1)

    lanes = 128
    recv_rows = lax.all_to_all(
        jnp.broadcast_to(slot_table.astype(jnp.int32)[:, None], (ntiles, lanes)),
        "tiles", 0, 0, tiled=True,
    )

    picked = jnp.minimum(recv_rows[:, 0], owned - 1)
    slot_ids = jnp.arange(owned, dtype=jnp.int32)
    holder = jnp.sum(
        jnp.where(recv_rows[:, :owned] == slot_ids[None, :], tile_ids[:, None], 0), axis=0
    )

    local = observed.reshape(day_count, owned, ndays, quarter)
    outgoing = jnp.take(local, picked, axis=1, mode="clip")
    outgoing = outgoing.transpose(1, 2, 0, 3).reshape(ntiles * ndays, day_count, quarter)
    arrived = lax.all_to_all(outgoing, ("tiles", "days"), 0, 0, tiled=True)
    arrived = arrived.reshape(ntiles, ndays * day_count, quarter)
    own_rows = jnp.take(arrived, target, axis=0, mode="clip")

    mapped_part = quantile_map(own_rows, knot_base, knot_steps)

    packed = jnp.take(mapped_part, local_of, axis=0, mode="clip")
    packed = packed.reshape(ntiles * ndays, day_count, quarter)
    returned = lax.all_to_all(packed, ("tiles", "days"), 0, 0, tiled=True)
    returned = returned.reshape(ntiles, ndays, day_count, quarter)
    blocks = jnp.take(returned, holder, axis=0, mode="clip")
    mapped = blocks.transpose(2, 0, 1, 3).reshape(day_count, row_count, columns)

    depth = PASSES
    weights = terrain * land_mask.astype(jnp.float32)
    wide_maps = with_halo(jnp.stack([weights, terrain]), depth)
    wide_weights = wide_maps[0]
    wide_center = center_share * wide_maps[1]
    wide_denom = wide_center + neighbour_sum(jnp.pad(wide_weights, 1))
    wide_denom = jnp.where(wide_denom > 0.0, wide_denom, 1.0)
    wide_field = with_halo(mapped, depth).astype(jnp.float32)
    for sweep in range(PASSES):
        padded = jnp.pad(wide_field * wide_weights[None], ((0, 0), (1, 1), (1, 1)))
        wide_field = (wide_center[None] * wide_field + neighbour_sum(padded)) / wide_denom[None]
    return wide_field[:, depth : depth + row_count, :]


def solution(mesh):
    return jax.shard_map(
        body,
        mesh=mesh,
        in_specs=(
            P("days", "tiles", None),
            P("tiles", None, "days"),
            P("tiles", None, None, "days"),
            P("tiles"),
            P("tiles", None),
            P("tiles", None),
        ),
        out_specs=P("days", "tiles", None),
        check_vma=False,
    )
```

```python
import jax
import jax.numpy as jnp
from jax import lax
from jax.sharding import PartitionSpec as P

PASSES = 4


center_share = 0.5


def neighbour_sum(padded):
    return (
        padded[..., :-2, 1:-1]
        + padded[..., 2:, 1:-1]
        + padded[..., 1:-1, :-2]
        + padded[..., 1:-1, 2:]
    )


def smoothed(field, weights, center, denom):
    for sweep in range(PASSES):
        padded = jnp.pad(field * weights[None], ((0, 0), (1, 1), (1, 1)))
        field = (center[None] * field + neighbour_sum(padded)) / denom[None]
    return field


def with_halo(cells, width):
    count = lax.axis_size("tiles")
    head = cells[..., :width, :]
    tail = cells[..., cells.shape[-2] - width :, :]
    from_above = lax.ppermute(tail, "tiles", [(i, i + 1) for i in range(count - 1)])
    from_below = lax.ppermute(head, "tiles", [(i + 1, i) for i in range(count - 1)])
    return jnp.concatenate([from_above, cells, from_below], axis=-2)


def quantile_map(values, anchor, increments):
    step_x = increments[:, 0].astype(jnp.float32)
    step_y = increments[:, 1].astype(jnp.float32)
    position = anchor[:, 0][:, None, :].astype(jnp.float32) + jnp.cumsum(step_x, axis=1) - step_x
    upper = position + step_x
    slopes = step_y / step_x
    offset = anchor[:, 1].astype(jnp.float32) - jnp.sum(slopes * position, axis=1)
    clamped = jnp.minimum(
        jnp.maximum(values.astype(jnp.float32)[:, :, None, :], position[:, None]), upper[:, None]
    )
    total = jnp.sum(slopes[:, None] * clamped, axis=2)
    return (offset[:, None, :] + total).astype(jnp.bfloat16)


def body(observed, knot_base, knot_steps, block_route, land_mask, terrain):
    day_count, row_count, columns = observed.shape
    ntiles = lax.axis_size("tiles")
    ndays = lax.axis_size("days")
    owned = row_count // 2
    quarter = knot_base.shape[2]
    served = block_route.shape[0]
    tile_ids = jnp.arange(ntiles, dtype=jnp.int32)

    target = block_route // owned
    place_slot = block_route % owned
    match = target[None, :] == tile_ids[:, None]
    has = jnp.any(match, axis=1)
    slot_table = jnp.where(has, jnp.sum(jnp.where(match, place_slot[None, :], 0), axis=1), owned)
    local_of = jnp.sum(jnp.where(match, jnp.arange(served, dtype=jnp.int32)[None, :], 0), axis=1)

    lanes = 128
    recv_rows = lax.all_to_all(
        jnp.broadcast_to(slot_table.astype(jnp.int32)[:, None], (ntiles, lanes)),
        "tiles", 0, 0, tiled=True,
    )

    picked = jnp.minimum(recv_rows[:, 0], owned - 1)
    slot_ids = jnp.arange(owned, dtype=jnp.int32)
    holder = jnp.sum(
        jnp.where(recv_rows[:, :owned] == slot_ids[None, :], tile_ids[:, None], 0), axis=0
    )

    local = observed.reshape(day_count, owned, ndays, quarter)
    outgoing = jnp.take(local, picked, axis=1, mode="clip")
    outgoing = outgoing.transpose(1, 2, 0, 3).reshape(ntiles * ndays, day_count, quarter)
    arrived = lax.all_to_all(outgoing, ("tiles", "days"), 0, 0, tiled=True)
    arrived = arrived.reshape(ntiles, ndays * day_count, quarter)
    own_rows = jnp.take(arrived, target, axis=0, mode="clip")

    mapped_part = quantile_map(own_rows, knot_base, knot_steps)

    packed = jnp.take(mapped_part, local_of, axis=0, mode="clip")
    packed = packed.reshape(ntiles * ndays, day_count, quarter)
    returned = lax.all_to_all(packed, ("tiles", "days"), 0, 0, tiled=True)
    returned = returned.reshape(ntiles, ndays, day_count, quarter)
    blocks = jnp.take(returned, holder, axis=0, mode="clip")
    mapped = blocks.transpose(2, 0, 1, 3).reshape(day_count, row_count, columns)

    depth = PASSES
    weights = terrain * land_mask.astype(jnp.float32)
    wide_maps = with_halo(jnp.stack([weights, terrain]), depth)
    wide_weights = wide_maps[0]
    wide_center = center_share * wide_maps[1]
    wide_denom = wide_center + neighbour_sum(jnp.pad(wide_weights, 1))
    wide_denom = jnp.where(wide_denom > 0.0, wide_denom, 1.0)
    own_weights = wide_weights[depth : depth + row_count]
    own_center = wide_center[depth : depth + row_count]
    own_denom = wide_denom[depth : depth + row_count]
    field = mapped.astype(jnp.float32)
    inner = smoothed(field, own_weights, own_center, own_denom)
    wide_field = with_halo(mapped, depth).astype(jnp.float32)
    strip = 3 * depth
    top = smoothed(
        wide_field[:, :strip], wide_weights[:strip], wide_center[:strip], wide_denom[:strip]
    )
    low = row_count + 2 * depth - strip
    bottom = smoothed(
        wide_field[:, low:], wide_weights[low:], wide_center[low:], wide_denom[low:]
    )
    return jnp.concatenate(
        [top[:, depth : 2 * depth], inner[:, depth : row_count - depth], bottom[:, depth : 2 * depth]],
        axis=1,
    )


def solution(mesh):
    return jax.shard_map(
        body,
        mesh=mesh,
        in_specs=(
            P("days", "tiles", None),
            P("tiles", None, "days"),
            P("tiles", None, None, "days"),
            P("tiles"),
            P("tiles", None),
            P("tiles", None),
        ),
        out_specs=P("days", "tiles", None),
        check_vma=False,
    )
```

```python
import jax
import jax.numpy as jnp
from jax import lax
from jax.sharding import PartitionSpec as P

PASSES = 4


center_share = 0.5


def neighbour_sum(padded):
    return (
        padded[..., :-2, 1:-1]
        + padded[..., 2:, 1:-1]
        + padded[..., 1:-1, :-2]
        + padded[..., 1:-1, 2:]
    )


def smoothed(field, weights, center, denom):
    for sweep in range(PASSES):
        padded = jnp.pad(field * weights[None], ((0, 0), (1, 1), (1, 1)))
        field = (center[None] * field + neighbour_sum(padded)) / denom[None]
    return field


def select_rows(pick, rows):
    return jnp.dot(pick, rows, preferred_element_type=jnp.float32).astype(jnp.bfloat16)


def with_halo(cells, width):
    count = lax.axis_size("tiles")
    head = cells[..., :width, :]
    tail = cells[..., cells.shape[-2] - width :, :]
    from_above = lax.ppermute(tail, "tiles", [(i, i + 1) for i in range(count - 1)])
    from_below = lax.ppermute(head, "tiles", [(i + 1, i) for i in range(count - 1)])
    return jnp.concatenate([from_above, cells, from_below], axis=-2)


def quantile_map(values, anchor, increments):
    step_x = increments[:, 0].astype(jnp.float32)
    step_y = increments[:, 1].astype(jnp.float32)
    position = anchor[:, 0][:, None, :].astype(jnp.float32) + jnp.cumsum(step_x, axis=1) - step_x
    upper = position + step_x
    slopes = step_y / step_x
    offset = anchor[:, 1].astype(jnp.float32) - jnp.sum(slopes * position, axis=1)
    clamped = jnp.minimum(
        jnp.maximum(values.astype(jnp.float32)[:, :, None, :], position[:, None]), upper[:, None]
    )
    total = jnp.sum(slopes[:, None] * clamped, axis=2)
    return (offset[:, None, :] + total).astype(jnp.bfloat16)


def body(observed, knot_base, knot_steps, block_route, land_mask, terrain):
    day_count, row_count, columns = observed.shape
    ntiles = lax.axis_size("tiles")
    ndays = lax.axis_size("days")
    owned = row_count // 2
    quarter = knot_base.shape[2]
    served = block_route.shape[0]
    tile_ids = jnp.arange(ntiles, dtype=jnp.int32)

    target = block_route // owned
    place_slot = block_route % owned
    match = target[None, :] == tile_ids[:, None]
    has = jnp.any(match, axis=1)
    slot_table = jnp.where(has, jnp.sum(jnp.where(match, place_slot[None, :], 0), axis=1), owned)

    lanes = 128
    recv_rows = lax.all_to_all(
        jnp.broadcast_to(slot_table.astype(jnp.int32)[:, None], (ntiles, lanes)),
        "tiles", 0, 0, tiled=True,
    )

    slot_ids = jnp.arange(owned, dtype=jnp.int32)
    holder = jnp.sum(
        jnp.where(recv_rows[:, :owned] == slot_ids[None, :], tile_ids[:, None], 0), axis=0
    )

    send_pick = (recv_rows[:, :owned] == slot_ids[None, :]).astype(jnp.bfloat16)
    local = observed.reshape(day_count, owned, ndays, quarter).transpose(1, 2, 0, 3)
    outgoing = select_rows(send_pick, local.reshape(owned, -1))
    outgoing = outgoing.reshape(ntiles * ndays, day_count, quarter)
    arrived = lax.all_to_all(outgoing, ("tiles", "days"), 0, 0, tiled=True)
    arrived = arrived.reshape(ntiles, ndays * day_count * quarter)
    own_pick = match.T.astype(jnp.bfloat16)
    own_rows = select_rows(own_pick, arrived).reshape(served, ndays * day_count, quarter)

    mapped_part = quantile_map(own_rows, knot_base, knot_steps)

    packed = select_rows(match.astype(jnp.bfloat16), mapped_part.reshape(served, -1))
    packed = packed.reshape(ntiles * ndays, day_count, quarter)
    returned = lax.all_to_all(packed, ("tiles", "days"), 0, 0, tiled=True)
    returned = returned.reshape(ntiles, ndays, day_count, quarter)
    blocks = jnp.take(returned, holder, axis=0, mode="clip")
    mapped = blocks.transpose(2, 0, 1, 3).reshape(day_count, row_count, columns)

    depth = PASSES
    weights = terrain * land_mask.astype(jnp.float32)
    wide_maps = with_halo(jnp.stack([weights, terrain]), depth)
    wide_weights = wide_maps[0]
    wide_center = center_share * wide_maps[1]
    wide_denom = wide_center + neighbour_sum(jnp.pad(wide_weights, 1))
    wide_denom = jnp.where(wide_denom > 0.0, wide_denom, 1.0)
    own_weights = wide_weights[depth : depth + row_count]
    own_center = wide_center[depth : depth + row_count]
    own_denom = wide_denom[depth : depth + row_count]
    field = mapped.astype(jnp.float32)
    inner = smoothed(field, own_weights, own_center, own_denom)
    wide_field = with_halo(mapped, depth).astype(jnp.float32)
    strip = 3 * depth
    top = smoothed(
        wide_field[:, :strip], wide_weights[:strip], wide_center[:strip], wide_denom[:strip]
    )
    low = row_count + 2 * depth - strip
    bottom = smoothed(
        wide_field[:, low:], wide_weights[low:], wide_center[low:], wide_denom[low:]
    )
    return jnp.concatenate(
        [top[:, depth : 2 * depth], inner[:, depth : row_count - depth], bottom[:, depth : 2 * depth]],
        axis=1,
    )


def solution(mesh):
    return jax.shard_map(
        body,
        mesh=mesh,
        in_specs=(
            P("days", "tiles", None),
            P("tiles", None, "days"),
            P("tiles", None, None, "days"),
            P("tiles"),
            P("tiles", None),
            P("tiles", None),
        ),
        out_specs=P("days", "tiles", None),
        check_vma=False,
    )
```

```python
import jax
import jax.numpy as jnp
from jax import lax
from jax.sharding import PartitionSpec as P

PASSES = 4


center_share = 0.5


def neighbour_sum(padded):
    return (
        padded[..., :-2, 1:-1]
        + padded[..., 2:, 1:-1]
        + padded[..., 1:-1, :-2]
        + padded[..., 1:-1, 2:]
    )


def smoothed(field, weights, center, denom):
    for sweep in range(PASSES):
        padded = jnp.pad(field * weights[None], ((0, 0), (1, 1), (1, 1)))
        field = (center[None] * field + neighbour_sum(padded)) / denom[None]
    return field


def with_halo(cells, width):
    count = lax.axis_size("tiles")
    head = cells[..., :width, :]
    tail = cells[..., cells.shape[-2] - width :, :]
    from_above = lax.ppermute(tail, "tiles", [(i, i + 1) for i in range(count - 1)])
    from_below = lax.ppermute(head, "tiles", [(i + 1, i) for i in range(count - 1)])
    return jnp.concatenate([from_above, cells, from_below], axis=-2)


def quantile_map(values, anchor, increments):
    step_x = increments[:, 0].astype(jnp.float32)
    step_y = increments[:, 1].astype(jnp.float32)
    ends = anchor[:, 0][:, None, :].astype(jnp.float32) + jnp.cumsum(step_x, axis=1)
    position = jnp.concatenate([anchor[:, 0][:, None, :].astype(jnp.float32), ends], axis=1)
    slopes = step_y / step_x
    zero = jnp.zeros_like(slopes[:, :1])
    bends = jnp.concatenate([slopes, zero], axis=1) - jnp.concatenate([zero, slopes], axis=1)
    offset = anchor[:, 1].astype(jnp.float32) - jnp.sum(bends * position, axis=1)
    above = jnp.maximum(values.astype(jnp.float32)[:, :, None, :], position[:, None])
    total = jnp.sum(bends[:, None] * above, axis=2)
    return (offset[:, None, :] + total).astype(jnp.bfloat16)


def body(observed, knot_base, knot_steps, block_route, land_mask, terrain):
    day_count, row_count, columns = observed.shape
    ntiles = lax.axis_size("tiles")
    ndays = lax.axis_size("days")
    owned = row_count // 2
    quarter = knot_base.shape[2]
    served = block_route.shape[0]
    tile_ids = jnp.arange(ntiles, dtype=jnp.int32)

    target = block_route // owned
    place_slot = block_route % owned
    match = target[None, :] == tile_ids[:, None]
    has = jnp.any(match, axis=1)
    slot_table = jnp.where(has, jnp.sum(jnp.where(match, place_slot[None, :], 0), axis=1), owned)
    local_of = jnp.sum(jnp.where(match, jnp.arange(served, dtype=jnp.int32)[None, :], 0), axis=1)

    lanes = 128
    recv_rows = lax.all_to_all(
        jnp.broadcast_to(slot_table.astype(jnp.int32)[:, None], (ntiles, lanes)),
        "tiles", 0, 0, tiled=True,
    )

    picked = jnp.minimum(recv_rows[:, 0], owned - 1)
    slot_ids = jnp.arange(owned, dtype=jnp.int32)
    holder = jnp.sum(
        jnp.where(recv_rows[:, :owned] == slot_ids[None, :], tile_ids[:, None], 0), axis=0
    )

    local = observed.reshape(day_count, owned, ndays, quarter)
    outgoing = jnp.take(local, picked, axis=1, mode="clip")
    outgoing = outgoing.transpose(1, 2, 0, 3).reshape(ntiles * ndays, day_count, quarter)
    arrived = lax.all_to_all(outgoing, ("tiles", "days"), 0, 0, tiled=True)
    arrived = arrived.reshape(ntiles, ndays * day_count, quarter)
    own_rows = jnp.take(arrived, target, axis=0, mode="clip")

    mapped_part = quantile_map(own_rows, knot_base, knot_steps)

    packed = jnp.take(mapped_part, local_of, axis=0, mode="clip")
    packed = packed.reshape(ntiles * ndays, day_count, quarter)
    returned = lax.all_to_all(packed, ("tiles", "days"), 0, 0, tiled=True)
    returned = returned.reshape(ntiles, ndays, day_count, quarter)
    blocks = jnp.take(returned, holder, axis=0, mode="clip")
    mapped = blocks.transpose(2, 0, 1, 3).reshape(day_count, row_count, columns)

    depth = PASSES
    weights = terrain * land_mask.astype(jnp.float32)
    wide_maps = with_halo(jnp.stack([weights, terrain]), depth)
    wide_weights = wide_maps[0]
    wide_center = center_share * wide_maps[1]
    wide_denom = wide_center + neighbour_sum(jnp.pad(wide_weights, 1))
    wide_denom = jnp.where(wide_denom > 0.0, wide_denom, 1.0)
    own_weights = wide_weights[depth : depth + row_count]
    own_center = wide_center[depth : depth + row_count]
    own_denom = wide_denom[depth : depth + row_count]
    field = mapped.astype(jnp.float32)
    inner = smoothed(field, own_weights, own_center, own_denom)
    wide_field = with_halo(mapped, depth).astype(jnp.float32)
    strip = 3 * depth
    top = smoothed(
        wide_field[:, :strip], wide_weights[:strip], wide_center[:strip], wide_denom[:strip]
    )
    low = row_count + 2 * depth - strip
    bottom = smoothed(
        wide_field[:, low:], wide_weights[low:], wide_center[low:], wide_denom[low:]
    )
    inner = lax.dynamic_update_slice_in_dim(inner, top[:, depth : 2 * depth], 0, axis=1)
    return lax.dynamic_update_slice_in_dim(
        inner, bottom[:, depth : 2 * depth], row_count - depth, axis=1
    )


def solution(mesh):
    return jax.shard_map(
        body,
        mesh=mesh,
        in_specs=(
            P("days", "tiles", None),
            P("tiles", None, "days"),
            P("tiles", None, None, "days"),
            P("tiles"),
            P("tiles", None),
            P("tiles", None),
        ),
        out_specs=P("days", "tiles", None),
        check_vma=False,
    )
```

```python
import jax
import jax.numpy as jnp
from jax import lax
from jax.sharding import PartitionSpec as P

PASSES = 4


center_share = 0.5


def neighbour_sum(padded):
    return (
        padded[..., :-2, 1:-1]
        + padded[..., 2:, 1:-1]
        + padded[..., 1:-1, :-2]
        + padded[..., 1:-1, 2:]
    )


def smoothed(field, weights, center, denom):
    for sweep in range(PASSES):
        padded = jnp.pad(field * weights[None], ((0, 0), (1, 1), (1, 1)))
        field = (center[None] * field + neighbour_sum(padded)) / denom[None]
    return field


def with_halo(cells, width, edge_rows=None):
    count = lax.axis_size("tiles")
    if edge_rows is None:
        edge_rows = jnp.concatenate([cells[..., :width, :], cells[..., cells.shape[-2] - width :, :]], axis=-2)
    head = edge_rows[..., :width, :]
    tail = edge_rows[..., width:, :]
    from_above = lax.ppermute(tail, "tiles", [(i, i + 1) for i in range(count - 1)])
    from_below = lax.ppermute(head, "tiles", [(i + 1, i) for i in range(count - 1)])
    return jnp.concatenate([from_above, cells, from_below], axis=-2)


def quantile_map(values, anchor, increments):
    step_x = increments[:, 0].astype(jnp.float32)
    step_y = increments[:, 1].astype(jnp.float32)
    ends = anchor[:, 0][:, None, :].astype(jnp.float32) + jnp.cumsum(step_x, axis=1)
    position = jnp.concatenate([anchor[:, 0][:, None, :].astype(jnp.float32), ends], axis=1)
    slopes = step_y / step_x
    zero = jnp.zeros_like(slopes[:, :1])
    bends = jnp.concatenate([slopes, zero], axis=1) - jnp.concatenate([zero, slopes], axis=1)
    offset = anchor[:, 1].astype(jnp.float32) - jnp.sum(bends * position, axis=1)
    above = jnp.maximum(values.astype(jnp.float32)[:, :, None, :], position[:, None])
    total = jnp.sum(bends[:, None] * above, axis=2)
    return (offset[:, None, :] + total).astype(jnp.bfloat16)


def body(observed, knot_base, knot_steps, block_route, land_mask, terrain):
    day_count, row_count, columns = observed.shape
    ntiles = lax.axis_size("tiles")
    ndays = lax.axis_size("days")
    owned = row_count // 2
    quarter = knot_base.shape[2]
    served = block_route.shape[0]
    tile_ids = jnp.arange(ntiles, dtype=jnp.int32)

    target = block_route // owned
    place_slot = block_route % owned
    match = target[None, :] == tile_ids[:, None]
    has = jnp.any(match, axis=1)
    slot_table = jnp.where(has, jnp.sum(jnp.where(match, place_slot[None, :], 0), axis=1), owned)
    local_of = jnp.sum(jnp.where(match, jnp.arange(served, dtype=jnp.int32)[None, :], 0), axis=1)

    lanes = 128
    recv_rows = lax.all_to_all(
        jnp.broadcast_to(slot_table.astype(jnp.int32)[:, None], (ntiles, lanes)),
        "tiles", 0, 0, tiled=True,
    )

    picked = jnp.minimum(recv_rows[:, 0], owned - 1)
    slot_ids = jnp.arange(owned, dtype=jnp.int32)
    holder = jnp.sum(
        jnp.where(recv_rows[:, :owned] == slot_ids[None, :], tile_ids[:, None], 0), axis=0
    )

    local = observed.reshape(day_count, owned, ndays, quarter)
    outgoing = jnp.take(local, picked, axis=1, mode="clip")
    outgoing = outgoing.transpose(1, 2, 0, 3).reshape(ntiles * ndays, day_count, quarter)
    arrived = lax.all_to_all(outgoing, ("tiles", "days"), 0, 0, tiled=True)
    arrived = arrived.reshape(ntiles, ndays * day_count, quarter)
    own_rows = jnp.take(arrived, target, axis=0, mode="clip")

    mapped_part = quantile_map(own_rows, knot_base, knot_steps)

    packed = jnp.take(mapped_part, local_of, axis=0, mode="clip")
    packed = packed.reshape(ntiles * ndays, day_count, quarter)
    returned = lax.all_to_all(packed, ("tiles", "days"), 0, 0, tiled=True)
    returned = returned.reshape(ntiles, ndays, day_count, quarter)
    blocks = jnp.take(returned, holder, axis=0, mode="clip")
    mapped = blocks.transpose(2, 0, 1, 3).reshape(day_count, row_count, columns)
    edge_count = PASSES // 2
    edges = jnp.concatenate([holder[:edge_count], holder[owned - edge_count :]])
    edge_rows = jnp.take(returned, edges, axis=0, mode="clip").transpose(2, 0, 1, 3)
    edge_rows = edge_rows.reshape(day_count, 2 * PASSES, columns)

    depth = PASSES
    weights = terrain * land_mask.astype(jnp.float32)
    wide_maps = with_halo(jnp.stack([weights, terrain]), depth)
    wide_weights = wide_maps[0]
    wide_center = center_share * wide_maps[1]
    wide_denom = wide_center + neighbour_sum(jnp.pad(wide_weights, 1))
    wide_denom = jnp.where(wide_denom > 0.0, wide_denom, 1.0)
    own_weights = wide_weights[depth : depth + row_count]
    own_center = wide_center[depth : depth + row_count]
    own_denom = wide_denom[depth : depth + row_count]
    field = mapped.astype(jnp.float32)
    inner = smoothed(field, own_weights, own_center, own_denom)
    wide_field = with_halo(mapped, depth, edge_rows).astype(jnp.float32)
    strip = 3 * depth
    top = smoothed(
        wide_field[:, :strip], wide_weights[:strip], wide_center[:strip], wide_denom[:strip]
    )
    low = row_count + 2 * depth - strip
    bottom = smoothed(
        wide_field[:, low:], wide_weights[low:], wide_center[low:], wide_denom[low:]
    )
    return jnp.concatenate(
        [top[:, depth : 2 * depth], inner[:, depth : row_count - depth], bottom[:, depth : 2 * depth]],
        axis=1,
    )


def solution(mesh):
    return jax.shard_map(
        body,
        mesh=mesh,
        in_specs=(
            P("days", "tiles", None),
            P("tiles", None, "days"),
            P("tiles", None, None, "days"),
            P("tiles"),
            P("tiles", None),
            P("tiles", None),
        ),
        out_specs=P("days", "tiles", None),
        check_vma=False,
    )
```

```python
import jax
import jax.numpy as jnp
from jax import lax
from jax.sharding import PartitionSpec as P

PASSES = 4


center_share = 0.5


def neighbour_sum(padded):
    return (
        padded[..., :-2, 1:-1]
        + padded[..., 2:, 1:-1]
        + padded[..., 1:-1, :-2]
        + padded[..., 1:-1, 2:]
    )


def smoothed(field, weights, center, denom):
    for sweep in range(PASSES):
        padded = jnp.pad(field * weights[None], ((0, 0), (1, 1), (1, 1)))
        field = (center[None] * field + neighbour_sum(padded)) / denom[None]
    return field


def with_halo(cells, width, edge_rows=None):
    count = lax.axis_size("tiles")
    if edge_rows is None:
        edge_rows = jnp.concatenate([cells[..., :width, :], cells[..., cells.shape[-2] - width :, :]], axis=-2)
    head = edge_rows[..., :width, :]
    tail = edge_rows[..., width:, :]
    from_above = lax.ppermute(tail, "tiles", [(i, i + 1) for i in range(count - 1)])
    from_below = lax.ppermute(head, "tiles", [(i + 1, i) for i in range(count - 1)])
    return jnp.concatenate([from_above, cells, from_below], axis=-2)


def quantile_map(values, anchor, increments):
    step_x = increments[:, 0].astype(jnp.float32)
    step_y = increments[:, 1].astype(jnp.float32)
    ends = anchor[:, 0][:, None, :].astype(jnp.float32) + jnp.cumsum(step_x, axis=1)
    position = jnp.concatenate([anchor[:, 0][:, None, :].astype(jnp.float32), ends], axis=1)
    slopes = step_y / step_x
    zero = jnp.zeros_like(slopes[:, :1])
    bends = jnp.concatenate([slopes, zero], axis=1) - jnp.concatenate([zero, slopes], axis=1)
    offset = anchor[:, 1].astype(jnp.float32) - jnp.sum(bends * position, axis=1)
    above = jnp.maximum(values.astype(jnp.float32)[:, :, None, :], position[:, None])
    total = jnp.sum(bends[:, None] * above, axis=2)
    return (offset[:, None, :] + total).astype(jnp.bfloat16)


def body(observed, knot_base, knot_steps, block_route, land_mask, terrain):
    day_count, row_count, columns = observed.shape
    ntiles = lax.axis_size("tiles")
    ndays = lax.axis_size("days")
    owned = row_count // 2
    quarter = knot_base.shape[2]
    served = block_route.shape[0]
    tile_ids = jnp.arange(ntiles, dtype=jnp.int32)

    target = block_route // owned
    place_slot = block_route % owned
    match = target[None, :] == tile_ids[:, None]
    has = jnp.any(match, axis=1)
    slot_table = jnp.where(has, jnp.sum(jnp.where(match, place_slot[None, :], 0), axis=1), owned)

    lanes = 128
    recv_rows = lax.all_to_all(
        jnp.broadcast_to(slot_table.astype(jnp.int32)[:, None], (ntiles, lanes)),
        "tiles", 0, 0, tiled=True,
    )

    picked = jnp.minimum(recv_rows[:, 0], owned - 1)
    slot_ids = jnp.arange(owned, dtype=jnp.int32)
    holder = jnp.sum(
        jnp.where(recv_rows[:, :owned] == slot_ids[None, :], tile_ids[:, None], 0), axis=0
    )

    local = observed.reshape(day_count, owned, ndays, quarter)
    outgoing = jnp.take(local, picked, axis=1, mode="clip")
    outgoing = outgoing.transpose(1, 2, 0, 3).reshape(ntiles * ndays, day_count, quarter)
    arrived = lax.all_to_all(outgoing, ("tiles", "days"), 0, 0, tiled=True)
    arrived = arrived.reshape(ntiles, ndays * day_count, quarter)
    own_rows = jnp.take(arrived, target, axis=0, mode="clip")

    mapped_part = quantile_map(own_rows, knot_base, knot_steps)

    packed = arrived.at[target].set(mapped_part, unique_indices=True, mode="promise_in_bounds")
    packed = packed.reshape(ntiles * ndays, day_count, quarter)
    returned = lax.all_to_all(packed, ("tiles", "days"), 0, 0, tiled=True)
    returned = returned.reshape(ntiles, ndays, day_count, quarter)
    blocks = jnp.take(returned, holder, axis=0, mode="clip")
    mapped = blocks.transpose(2, 0, 1, 3).reshape(day_count, row_count, columns)
    edge_count = PASSES // 2
    edges = jnp.concatenate([holder[:edge_count], holder[owned - edge_count :]])
    edge_rows = jnp.take(returned, edges, axis=0, mode="clip").transpose(2, 0, 1, 3)
    edge_rows = edge_rows.reshape(day_count, 2 * PASSES, columns)

    depth = PASSES
    weights = terrain * land_mask.astype(jnp.float32)
    wide_maps = with_halo(jnp.stack([weights, terrain]), depth)
    wide_weights = wide_maps[0]
    wide_center = center_share * wide_maps[1]
    wide_denom = wide_center + neighbour_sum(jnp.pad(wide_weights, 1))
    wide_denom = jnp.where(wide_denom > 0.0, wide_denom, 1.0)
    own_weights = wide_weights[depth : depth + row_count]
    own_center = wide_center[depth : depth + row_count]
    own_denom = wide_denom[depth : depth + row_count]
    field = mapped.astype(jnp.float32)
    inner = smoothed(field, own_weights, own_center, own_denom)
    wide_field = with_halo(mapped, depth, edge_rows).astype(jnp.float32)
    strip = 3 * depth
    top = smoothed(
        wide_field[:, :strip], wide_weights[:strip], wide_center[:strip], wide_denom[:strip]
    )
    low = row_count + 2 * depth - strip
    bottom = smoothed(
        wide_field[:, low:], wide_weights[low:], wide_center[low:], wide_denom[low:]
    )
    return jnp.concatenate(
        [top[:, depth : 2 * depth], inner[:, depth : row_count - depth], bottom[:, depth : 2 * depth]],
        axis=1,
    )


def solution(mesh):
    return jax.shard_map(
        body,
        mesh=mesh,
        in_specs=(
            P("days", "tiles", None),
            P("tiles", None, "days"),
            P("tiles", None, None, "days"),
            P("tiles"),
            P("tiles", None),
            P("tiles", None),
        ),
        out_specs=P("days", "tiles", None),
        check_vma=False,
    )
```

```python
import jax
import jax.numpy as jnp
from jax import lax
from jax.experimental import pallas as pl
from jax.experimental.pallas import tpu as pltpu
from jax.sharding import PartitionSpec as P

PASSES = 4


center_share = 0.5


def neighbour_sum(padded):
    return (
        padded[..., :-2, 1:-1]
        + padded[..., 2:, 1:-1]
        + padded[..., 1:-1, :-2]
        + padded[..., 1:-1, 2:]
    )


def smoothed(field, weights, center, denom):
    for sweep in range(PASSES):
        padded = jnp.pad(field * weights[None], ((0, 0), (1, 1), (1, 1)))
        field = (center[None] * field + neighbour_sum(padded)) / denom[None]
    return field


def with_halo(cells, width, edge_rows=None):
    count = lax.axis_size("tiles")
    if edge_rows is None:
        edge_rows = jnp.concatenate([cells[..., :width, :], cells[..., cells.shape[-2] - width :, :]], axis=-2)
    head = edge_rows[..., :width, :]
    tail = edge_rows[..., width:, :]
    from_above = lax.ppermute(tail, "tiles", [(i, i + 1) for i in range(count - 1)])
    from_below = lax.ppermute(head, "tiles", [(i + 1, i) for i in range(count - 1)])
    return jnp.concatenate([from_above, cells, from_below], axis=-2)


def _qmap_kernel(tgt_ref, arrived_hbm, base_ref, steps_ref, out_hbm, vin, vout, sem_in, sem_out):
    served = vin.shape[0]
    knots = steps_ref.shape[2]
    for k in range(served):
        pltpu.make_async_copy(arrived_hbm.at[tgt_ref[k]], vin.at[k], sem_in.at[k]).start()
    for k in range(served):
        pltpu.make_async_copy(arrived_hbm.at[tgt_ref[k]], vin.at[k], sem_in.at[k]).wait()

    def block(k, carry):
        x = vin[k].astype(jnp.float32)
        step_x = steps_ref[k, 0].astype(jnp.float32)
        step_y = steps_ref[k, 1].astype(jnp.float32)
        slopes = step_y / step_x
        p = base_ref[k, 0:1, :].astype(jnp.float32)
        offset = base_ref[k, 1:2, :].astype(jnp.float32)
        acc = jnp.zeros_like(x)
        before = jnp.zeros_like(p)
        for j in range(knots + 1):
            now = slopes[j : j + 1] if j < knots else jnp.zeros_like(p)
            bend = now - before
            acc = acc + bend * jnp.maximum(x, p)
            offset = offset - bend * p
            if j < knots:
                p = p + step_x[j : j + 1]
            before = now
        vout[k] = (offset + acc).astype(vout.dtype)
        return carry

    lax.fori_loop(0, served, block, 0)
    for k in range(served):
        pltpu.make_async_copy(vout.at[k], out_hbm.at[tgt_ref[k]], sem_out.at[k]).start()
    for k in range(served):
        pltpu.make_async_copy(vout.at[k], out_hbm.at[tgt_ref[k]], sem_out.at[k]).wait()


def mapped_rows(target, arrived, anchor, increments):
    served = anchor.shape[0]
    rows = arrived.shape[1:]
    return pl.pallas_call(
        _qmap_kernel,
        grid_spec=pltpu.PrefetchScalarGridSpec(
            num_scalar_prefetch=1,
            grid=(1,),
            in_specs=[
                pl.BlockSpec(memory_space=pl.ANY),
                pl.BlockSpec(anchor.shape, lambda i, t: (0, 0, 0)),
                pl.BlockSpec(increments.shape, lambda i, t: (0, 0, 0, 0)),
            ],
            out_specs=pl.BlockSpec(memory_space=pl.ANY),
            scratch_shapes=[
                pltpu.VMEM((served,) + rows, arrived.dtype),
                pltpu.VMEM((served,) + rows, jnp.bfloat16),
                pltpu.SemaphoreType.DMA((served,)),
                pltpu.SemaphoreType.DMA((served,)),
            ],
        ),
        out_shape=jax.ShapeDtypeStruct(arrived.shape, jnp.bfloat16),
    )(target, arrived, anchor, increments)

def body(observed, knot_base, knot_steps, block_route, land_mask, terrain):
    day_count, row_count, columns = observed.shape
    ntiles = lax.axis_size("tiles")
    ndays = lax.axis_size("days")
    owned = row_count // 2
    quarter = knot_base.shape[2]
    served = block_route.shape[0]
    tile_ids = jnp.arange(ntiles, dtype=jnp.int32)

    target = block_route // owned
    place_slot = block_route % owned
    match = target[None, :] == tile_ids[:, None]
    has = jnp.any(match, axis=1)
    slot_table = jnp.where(has, jnp.sum(jnp.where(match, place_slot[None, :], 0), axis=1), owned)

    lanes = 128
    recv_rows = lax.all_to_all(
        jnp.broadcast_to(slot_table.astype(jnp.int32)[:, None], (ntiles, lanes)),
        "tiles", 0, 0, tiled=True,
    )

    picked = jnp.minimum(recv_rows[:, 0], owned - 1)
    slot_ids = jnp.arange(owned, dtype=jnp.int32)
    holder = jnp.sum(
        jnp.where(recv_rows[:, :owned] == slot_ids[None, :], tile_ids[:, None], 0), axis=0
    )

    local = observed.reshape(day_count, owned, ndays, quarter)
    outgoing = jnp.take(local, picked, axis=1, mode="clip")
    outgoing = outgoing.transpose(1, 2, 0, 3).reshape(ntiles * ndays, day_count, quarter)
    arrived = lax.all_to_all(outgoing, ("tiles", "days"), 0, 0, tiled=True)
    arrived = arrived.reshape(ntiles, ndays * day_count, quarter)
    packed = mapped_rows(target, arrived, knot_base, knot_steps)
    packed = packed.reshape(ntiles * ndays, day_count, quarter)
    returned = lax.all_to_all(packed, ("tiles", "days"), 0, 0, tiled=True)
    returned = returned.reshape(ntiles, ndays, day_count, quarter)
    blocks = jnp.take(returned, holder, axis=0, mode="clip")
    mapped = blocks.transpose(2, 0, 1, 3).reshape(day_count, row_count, columns)
    edge_count = PASSES // 2
    edges = jnp.concatenate([holder[:edge_count], holder[owned - edge_count :]])
    edge_rows = jnp.take(returned, edges, axis=0, mode="clip").transpose(2, 0, 1, 3)
    edge_rows = edge_rows.reshape(day_count, 2 * PASSES, columns)

    depth = PASSES
    weights = terrain * land_mask.astype(jnp.float32)
    wide_maps = with_halo(jnp.stack([weights, terrain]), depth)
    wide_weights = wide_maps[0]
    wide_center = center_share * wide_maps[1]
    wide_denom = wide_center + neighbour_sum(jnp.pad(wide_weights, 1))
    wide_denom = jnp.where(wide_denom > 0.0, wide_denom, 1.0)
    own_weights = wide_weights[depth : depth + row_count]
    own_center = wide_center[depth : depth + row_count]
    own_denom = wide_denom[depth : depth + row_count]
    field = mapped.astype(jnp.float32)
    inner = smoothed(field, own_weights, own_center, own_denom)
    wide_field = with_halo(mapped, depth, edge_rows).astype(jnp.float32)
    strip = 3 * depth
    top = smoothed(
        wide_field[:, :strip], wide_weights[:strip], wide_center[:strip], wide_denom[:strip]
    )
    low = row_count + 2 * depth - strip
    bottom = smoothed(
        wide_field[:, low:], wide_weights[low:], wide_center[low:], wide_denom[low:]
    )
    return jnp.concatenate(
        [top[:, depth : 2 * depth], inner[:, depth : row_count - depth], bottom[:, depth : 2 * depth]],
        axis=1,
    )


def solution(mesh):
    return jax.shard_map(
        body,
        mesh=mesh,
        in_specs=(
            P("days", "tiles", None),
            P("tiles", None, "days"),
            P("tiles", None, None, "days"),
            P("tiles"),
            P("tiles", None),
            P("tiles", None),
        ),
        out_specs=P("days", "tiles", None),
        check_vma=False,
    )
```

```python
import jax
import jax.numpy as jnp
from jax import lax
from jax.sharding import PartitionSpec as P

PASSES = 4


center_share = 0.5


def neighbour_sum(padded):
    return (
        padded[..., :-2, 1:-1]
        + padded[..., 2:, 1:-1]
        + padded[..., 1:-1, :-2]
        + padded[..., 1:-1, 2:]
    )


def smoothed(field, weights, center, denom):
    for sweep in range(PASSES):
        padded = jnp.pad(field * weights[None], ((0, 0), (1, 1), (1, 1)))
        field = (center[None] * field + neighbour_sum(padded)) / denom[None]
    return field


def with_halo(cells, width, edge_rows=None):
    count = lax.axis_size("tiles")
    if edge_rows is None:
        edge_rows = jnp.concatenate([cells[..., :width, :], cells[..., cells.shape[-2] - width :, :]], axis=-2)
    head = edge_rows[..., :width, :]
    tail = edge_rows[..., width:, :]
    from_above = lax.ppermute(tail, "tiles", [(i, i + 1) for i in range(count - 1)])
    from_below = lax.ppermute(head, "tiles", [(i + 1, i) for i in range(count - 1)])
    return jnp.concatenate([from_above, cells, from_below], axis=-2)


def quantile_map(values, anchor, increments):
    step_x = increments[:, 0].astype(jnp.float32)
    step_y = increments[:, 1].astype(jnp.float32)
    ends = anchor[:, 0][:, None, :].astype(jnp.float32) + jnp.cumsum(step_x, axis=1)
    position = jnp.concatenate([anchor[:, 0][:, None, :].astype(jnp.float32), ends], axis=1)
    slopes = step_y / step_x
    zero = jnp.zeros_like(slopes[:, :1])
    bends = jnp.concatenate([slopes, zero], axis=1) - jnp.concatenate([zero, slopes], axis=1)
    offset = anchor[:, 1].astype(jnp.float32) - jnp.sum(bends * position, axis=1)
    above = jnp.maximum(values.astype(jnp.float32)[:, :, None, :], position[:, None])
    total = jnp.sum(bends[:, None] * above, axis=2)
    return (offset[:, None, :] + total).astype(jnp.bfloat16)


def body(observed, knot_base, knot_steps, block_route, land_mask, terrain):
    day_count, row_count, columns = observed.shape
    ntiles = lax.axis_size("tiles")
    ndays = lax.axis_size("days")
    owned = row_count // 2
    quarter = knot_base.shape[2]
    served = block_route.shape[0]
    tile_ids = jnp.arange(ntiles, dtype=jnp.int32)

    target = block_route // owned
    place_slot = block_route % owned
    match = target[None, :] == tile_ids[:, None]
    has = jnp.any(match, axis=1)
    slot_table = jnp.where(has, jnp.sum(jnp.where(match, place_slot[None, :], 0), axis=1), owned)
    local_of = jnp.sum(jnp.where(match, jnp.arange(served, dtype=jnp.int32)[None, :], 0), axis=1)

    lanes = 128
    recv_rows = lax.all_to_all(
        jnp.broadcast_to(slot_table.astype(jnp.int32)[:, None], (ntiles, lanes)),
        "tiles", 0, 0, tiled=True,
    )

    knots = jnp.concatenate([knot_base[:, :, None, :], knot_steps], axis=2)
    knots = lax.all_to_all(
        jnp.broadcast_to(knots[None], (ndays,) + knots.shape), "days", 0, 0, tiled=True
    )
    anchors = knots[:, :, :, 0, :]
    quarters = knots[:, :, :, 1:, :]

    picked = jnp.minimum(recv_rows[:, 0], owned - 1)
    slot_ids = jnp.arange(owned, dtype=jnp.int32)
    holder = jnp.sum(
        jnp.where(recv_rows[:, :owned] == slot_ids[None, :], tile_ids[:, None], 0), axis=0
    )

    local = observed.reshape(day_count, owned, 2 * columns)
    outgoing = jnp.take(local, picked, axis=1, mode="clip").transpose(1, 0, 2)
    arrived = lax.all_to_all(outgoing, "tiles", 0, 0, tiled=True)
    own_rows = jnp.take(arrived, target, axis=0, mode="clip")
    own_rows = own_rows.reshape(served, day_count, ndays, quarter).transpose(2, 0, 1, 3)

    mapped_part = quantile_map(
        own_rows.reshape(ndays * served, day_count, quarter),
        anchors.reshape(ndays * served, 2, quarter),
        quarters.reshape((ndays * served,) + knot_steps.shape[1:]),
    )
    mapped_part = mapped_part.reshape(ndays, served, day_count, quarter).transpose(1, 2, 0, 3)
    mapped_part = mapped_part.reshape(served, day_count, 2 * columns)

    packed = jnp.take(mapped_part, local_of, axis=0, mode="clip")
    returned = lax.all_to_all(packed, "tiles", 0, 0, tiled=True)
    blocks = jnp.take(returned, holder, axis=0, mode="clip")
    mapped = blocks.transpose(1, 0, 2).reshape(day_count, row_count, columns)
    edge_count = PASSES // 2
    edges = jnp.concatenate([holder[:edge_count], holder[owned - edge_count :]])
    edge_rows = jnp.take(returned, edges, axis=0, mode="clip").transpose(1, 0, 2)
    edge_rows = edge_rows.reshape(day_count, 2 * PASSES, columns)

    depth = PASSES
    weights = terrain * land_mask.astype(jnp.float32)
    wide_maps = with_halo(jnp.stack([weights, terrain]), depth)
    wide_weights = wide_maps[0]
    wide_center = center_share * wide_maps[1]
    wide_denom = wide_center + neighbour_sum(jnp.pad(wide_weights, 1))
    wide_denom = jnp.where(wide_denom > 0.0, wide_denom, 1.0)
    own_weights = wide_weights[depth : depth + row_count]
    own_center = wide_center[depth : depth + row_count]
    own_denom = wide_denom[depth : depth + row_count]
    field = mapped.astype(jnp.float32)
    inner = smoothed(field, own_weights, own_center, own_denom)
    wide_field = with_halo(mapped, depth, edge_rows).astype(jnp.float32)
    strip = 3 * depth
    top = smoothed(
        wide_field[:, :strip], wide_weights[:strip], wide_center[:strip], wide_denom[:strip]
    )
    low = row_count + 2 * depth - strip
    bottom = smoothed(
        wide_field[:, low:], wide_weights[low:], wide_center[low:], wide_denom[low:]
    )
    return jnp.concatenate(
        [top[:, depth : 2 * depth], inner[:, depth : row_count - depth], bottom[:, depth : 2 * depth]],
        axis=1,
    )


def solution(mesh):
    return jax.shard_map(
        body,
        mesh=mesh,
        in_specs=(
            P("days", "tiles", None),
            P("tiles", None, "days"),
            P("tiles", None, None, "days"),
            P("tiles"),
            P("tiles", None),
            P("tiles", None),
        ),
        out_specs=P("days", "tiles", None),
        check_vma=False,
    )
```

```python
import jax
import jax.numpy as jnp
from jax import lax
from jax.sharding import PartitionSpec as P

PASSES = 4


center_share = 0.5


def neighbour_sum(padded):
    return (
        padded[..., :-2, 1:-1]
        + padded[..., 2:, 1:-1]
        + padded[..., 1:-1, :-2]
        + padded[..., 1:-1, 2:]
    )


def smoothed(field, weights, center, denom):
    for sweep in range(PASSES):
        padded = jnp.pad(field * weights[None], ((0, 0), (1, 1), (1, 1)))
        field = (center[None] * field + neighbour_sum(padded)) / denom[None]
    return field


def with_halo(cells, width, edge_rows=None):
    count = lax.axis_size("tiles")
    if edge_rows is None:
        edge_rows = jnp.concatenate([cells[..., :width, :], cells[..., cells.shape[-2] - width :, :]], axis=-2)
    head = edge_rows[..., :width, :]
    tail = edge_rows[..., width:, :]
    from_above = lax.ppermute(tail, "tiles", [(i, i + 1) for i in range(count - 1)])
    from_below = lax.ppermute(head, "tiles", [(i + 1, i) for i in range(count - 1)])
    return jnp.concatenate([from_above, cells, from_below], axis=-2)


def quantile_map(values, anchor, increments):
    step_x = increments[:, 0].astype(jnp.float32)
    step_y = increments[:, 1].astype(jnp.float32)
    ends = anchor[:, 0][:, None, :].astype(jnp.float32) + jnp.cumsum(step_x, axis=1)
    position = jnp.concatenate([anchor[:, 0][:, None, :].astype(jnp.float32), ends], axis=1)
    slopes = step_y / step_x
    zero = jnp.zeros_like(slopes[:, :1])
    bends = jnp.concatenate([slopes, zero], axis=1) - jnp.concatenate([zero, slopes], axis=1)
    offset = anchor[:, 1].astype(jnp.float32) - jnp.sum(bends * position, axis=1)
    above = jnp.maximum(values.astype(jnp.float32)[:, :, None, :], position[:, None])
    total = jnp.sum(bends[:, None] * above, axis=2)
    return (offset[:, None, :] + total).astype(jnp.bfloat16)


def body(observed, knot_base, knot_steps, block_route, land_mask, terrain):
    day_count, row_count, columns = observed.shape
    ntiles = lax.axis_size("tiles")
    ndays = lax.axis_size("days")
    owned = row_count // 2
    quarter = knot_base.shape[2]
    served = block_route.shape[0]
    tile_ids = jnp.arange(ntiles, dtype=jnp.int32)

    target = block_route // owned
    place_slot = block_route % owned
    match = target[None, :] == tile_ids[:, None]
    has = jnp.any(match, axis=1)
    slot_table = jnp.where(has, jnp.sum(jnp.where(match, place_slot[None, :], 0), axis=1), owned)
    local_of = jnp.sum(jnp.where(match, jnp.arange(served, dtype=jnp.int32)[None, :], 0), axis=1)

    lanes = 128
    recv_rows = lax.all_to_all(
        jnp.broadcast_to(slot_table.astype(jnp.bfloat16)[:, None], (ntiles, lanes)),
        "tiles", 0, 0, tiled=True,
    )

    recv_rows = recv_rows.astype(jnp.int32)
    picked = jnp.minimum(recv_rows[:, 0], owned - 1)
    slot_ids = jnp.arange(owned, dtype=jnp.int32)
    holder = jnp.sum(
        jnp.where(recv_rows[:, :owned] == slot_ids[None, :], tile_ids[:, None], 0), axis=0
    )

    local = observed.reshape(day_count, owned, ndays, quarter).transpose(1, 2, 0, 3)
    local = lax.optimization_barrier(local)
    outgoing = jnp.take(local, picked, axis=0, mode="clip")
    outgoing = outgoing.reshape(ntiles * ndays, day_count, quarter)
    arrived = lax.all_to_all(outgoing, ("tiles", "days"), 0, 0, tiled=True)
    arrived = arrived.reshape(ntiles, ndays * day_count, quarter)
    own_rows = jnp.take(arrived, target, axis=0, mode="clip")

    mapped_part = quantile_map(own_rows, knot_base, knot_steps)

    packed = jnp.take(mapped_part, local_of, axis=0, mode="clip")
    packed = packed.reshape(ntiles * ndays, day_count, quarter)
    returned = lax.all_to_all(packed, ("tiles", "days"), 0, 0, tiled=True)
    returned = returned.reshape(ntiles, ndays, day_count, quarter)
    blocks = jnp.take(returned, holder, axis=0, mode="clip")
    mapped = blocks.transpose(2, 0, 1, 3).reshape(day_count, row_count, columns)
    edge_count = PASSES // 2
    edges = jnp.concatenate([holder[:edge_count], holder[owned - edge_count :]])
    edge_rows = jnp.take(returned, edges, axis=0, mode="clip").transpose(2, 0, 1, 3)
    edge_rows = edge_rows.reshape(day_count, 2 * PASSES, columns)

    depth = PASSES
    weights = terrain * land_mask.astype(jnp.float32)
    wide_maps = with_halo(jnp.stack([weights, terrain]), depth)
    wide_weights = wide_maps[0]
    wide_center = center_share * wide_maps[1]
    wide_denom = wide_center + neighbour_sum(jnp.pad(wide_weights, 1))
    wide_denom = jnp.where(wide_denom > 0.0, wide_denom, 1.0)
    own_weights = wide_weights[depth : depth + row_count]
    own_center = wide_center[depth : depth + row_count]
    own_denom = wide_denom[depth : depth + row_count]
    field = mapped.astype(jnp.float32)
    inner = smoothed(field, own_weights, own_center, own_denom)
    wide_field = with_halo(mapped, depth, edge_rows).astype(jnp.float32)
    strip = 3 * depth
    top = smoothed(
        wide_field[:, :strip], wide_weights[:strip], wide_center[:strip], wide_denom[:strip]
    )
    low = row_count + 2 * depth - strip
    bottom = smoothed(
        wide_field[:, low:], wide_weights[low:], wide_center[low:], wide_denom[low:]
    )
    return jnp.concatenate(
        [top[:, depth : 2 * depth], inner[:, depth : row_count - depth], bottom[:, depth : 2 * depth]],
        axis=1,
    )


def solution(mesh):
    return jax.shard_map(
        body,
        mesh=mesh,
        in_specs=(
            P("days", "tiles", None),
            P("tiles", None, "days"),
            P("tiles", None, None, "days"),
            P("tiles"),
            P("tiles", None),
            P("tiles", None),
        ),
        out_specs=P("days", "tiles", None),
        check_vma=False,
    )
```

```python
import jax
import jax.numpy as jnp
from jax import lax
from jax.experimental import pallas as pl
from jax.experimental.pallas import tpu as pltpu
from jax.sharding import PartitionSpec as P

PASSES = 4


center_share = 0.5


def neighbour_sum(padded):
    return (
        padded[..., :-2, 1:-1]
        + padded[..., 2:, 1:-1]
        + padded[..., 1:-1, :-2]
        + padded[..., 1:-1, 2:]
    )


def smoothed(field, weights, center, denom):
    for sweep in range(PASSES):
        padded = jnp.pad(field * weights[None], ((0, 0), (1, 1), (1, 1)))
        field = (center[None] * field + neighbour_sum(padded)) / denom[None]
    return field


def _place_kernel(dst_ref, src_hbm, out_hbm, sems):
    count = src_hbm.shape[0]
    for j in range(count):
        pltpu.make_async_copy(src_hbm.at[j], out_hbm.at[dst_ref[j]], sems.at[j]).start()
    for j in range(count):
        pltpu.make_async_copy(src_hbm.at[j], out_hbm.at[dst_ref[j]], sems.at[j]).wait()


def place_rows(dst, src, total):
    return pl.pallas_call(
        _place_kernel,
        grid_spec=pltpu.PrefetchScalarGridSpec(
            num_scalar_prefetch=1,
            grid=(1,),
            in_specs=[pl.BlockSpec(memory_space=pl.ANY)],
            out_specs=pl.BlockSpec(memory_space=pl.ANY),
            scratch_shapes=[pltpu.SemaphoreType.DMA((src.shape[0],))],
        ),
        out_shape=jax.ShapeDtypeStruct((total,) + src.shape[1:], src.dtype),
    )(dst, src)

def with_halo(cells, width, edge_rows=None):
    count = lax.axis_size("tiles")
    if edge_rows is None:
        edge_rows = jnp.concatenate([cells[..., :width, :], cells[..., cells.shape[-2] - width :, :]], axis=-2)
    head = edge_rows[..., :width, :]
    tail = edge_rows[..., width:, :]
    from_above = lax.ppermute(tail, "tiles", [(i, i + 1) for i in range(count - 1)])
    from_below = lax.ppermute(head, "tiles", [(i + 1, i) for i in range(count - 1)])
    return jnp.concatenate([from_above, cells, from_below], axis=-2)


def quantile_map(values, anchor, increments):
    step_x = increments[:, 0].astype(jnp.float32)
    step_y = increments[:, 1].astype(jnp.float32)
    ends = anchor[:, 0][:, None, :].astype(jnp.float32) + jnp.cumsum(step_x, axis=1)
    position = jnp.concatenate([anchor[:, 0][:, None, :].astype(jnp.float32), ends], axis=1)
    slopes = step_y / step_x
    zero = jnp.zeros_like(slopes[:, :1])
    bends = jnp.concatenate([slopes, zero], axis=1) - jnp.concatenate([zero, slopes], axis=1)
    offset = anchor[:, 1].astype(jnp.float32) - jnp.sum(bends * position, axis=1)
    above = jnp.maximum(values.astype(jnp.float32)[:, :, None, :], position[:, None])
    total = jnp.sum(bends[:, None] * above, axis=2)
    return (offset[:, None, :] + total).astype(jnp.bfloat16)


def body(observed, knot_base, knot_steps, block_route, land_mask, terrain):
    day_count, row_count, columns = observed.shape
    ntiles = lax.axis_size("tiles")
    ndays = lax.axis_size("days")
    owned = row_count // 2
    quarter = knot_base.shape[2]
    served = block_route.shape[0]
    tile_ids = jnp.arange(ntiles, dtype=jnp.int32)

    target = block_route // owned
    place_slot = block_route % owned
    match = target[None, :] == tile_ids[:, None]
    has = jnp.any(match, axis=1)
    slot_table = jnp.where(has, jnp.sum(jnp.where(match, place_slot[None, :], 0), axis=1), owned)

    lanes = 128
    recv_rows = lax.all_to_all(
        jnp.broadcast_to(slot_table.astype(jnp.bfloat16)[:, None], (ntiles, lanes)),
        "tiles", 0, 0, tiled=True,
    )

    recv_rows = recv_rows.astype(jnp.int32)
    slot_ids = jnp.arange(owned, dtype=jnp.int32)
    holder = jnp.sum(
        jnp.where(recv_rows[:, :owned] == slot_ids[None, :], tile_ids[:, None], 0), axis=0
    )

    local = observed.reshape(day_count, owned, ndays, quarter).transpose(1, 2, 0, 3)
    local = lax.optimization_barrier(local)
    outgoing = place_rows(holder, local.reshape(owned, ndays * day_count, quarter), ntiles)
    outgoing = outgoing.reshape(ntiles * ndays, day_count, quarter)
    arrived = lax.all_to_all(outgoing, ("tiles", "days"), 0, 0, tiled=True)
    arrived = arrived.reshape(ntiles, ndays * day_count, quarter)
    own_rows = jnp.take(arrived, target, axis=0, mode="clip")

    mapped_part = quantile_map(own_rows, knot_base, knot_steps)

    packed = place_rows(target, mapped_part, ntiles)
    packed = packed.reshape(ntiles * ndays, day_count, quarter)
    returned = lax.all_to_all(packed, ("tiles", "days"), 0, 0, tiled=True)
    returned = returned.reshape(ntiles, ndays, day_count, quarter)
    blocks = jnp.take(returned, holder, axis=0, mode="clip")
    mapped = blocks.transpose(2, 0, 1, 3).reshape(day_count, row_count, columns)
    edge_count = PASSES // 2
    edges = jnp.concatenate([holder[:edge_count], holder[owned - edge_count :]])
    edge_rows = jnp.take(returned, edges, axis=0, mode="clip").transpose(2, 0, 1, 3)
    edge_rows = edge_rows.reshape(day_count, 2 * PASSES, columns)

    depth = PASSES
    weights = terrain * land_mask.astype(jnp.float32)
    wide_maps = with_halo(jnp.stack([weights, terrain]), depth)
    wide_weights = wide_maps[0]
    wide_center = center_share * wide_maps[1]
    wide_denom = wide_center + neighbour_sum(jnp.pad(wide_weights, 1))
    wide_denom = jnp.where(wide_denom > 0.0, wide_denom, 1.0)
    own_weights = wide_weights[depth : depth + row_count]
    own_center = wide_center[depth : depth + row_count]
    own_denom = wide_denom[depth : depth + row_count]
    field = mapped.astype(jnp.float32)
    inner = smoothed(field, own_weights, own_center, own_denom)
    wide_field = with_halo(mapped, depth, edge_rows).astype(jnp.float32)
    strip = 3 * depth
    top = smoothed(
        wide_field[:, :strip], wide_weights[:strip], wide_center[:strip], wide_denom[:strip]
    )
    low = row_count + 2 * depth - strip
    bottom = smoothed(
        wide_field[:, low:], wide_weights[low:], wide_center[low:], wide_denom[low:]
    )
    return jnp.concatenate(
        [top[:, depth : 2 * depth], inner[:, depth : row_count - depth], bottom[:, depth : 2 * depth]],
        axis=1,
    )


def solution(mesh):
    return jax.shard_map(
        body,
        mesh=mesh,
        in_specs=(
            P("days", "tiles", None),
            P("tiles", None, "days"),
            P("tiles", None, None, "days"),
            P("tiles"),
            P("tiles", None),
            P("tiles", None),
        ),
        out_specs=P("days", "tiles", None),
        check_vma=False,
    )
```

```python
import jax
import jax.numpy as jnp
from jax import lax
from jax.sharding import PartitionSpec as P

PASSES = 4


center_share = 0.5


def neighbour_sum(padded):
    return (
        padded[..., :-2, 1:-1]
        + padded[..., 2:, 1:-1]
        + padded[..., 1:-1, :-2]
        + padded[..., 1:-1, 2:]
    )


def smoothed(field, weights, center, denom):
    for sweep in range(PASSES):
        padded = jnp.pad(field * weights[None], ((0, 0), (1, 1), (1, 1)))
        field = (center[None] * field + neighbour_sum(padded)) / denom[None]
    return field


def select_rows(pick, rows):
    depth = rows.shape[2]
    eye = jnp.eye(depth, dtype=pick.dtype)
    lhs = (pick[:, None, :, None] * eye[None, :, None, :]).reshape(pick.shape[0] * depth, -1)
    lhs = jnp.broadcast_to(lhs[None], (rows.shape[0],) + lhs.shape)
    flat = rows.reshape(rows.shape[0], rows.shape[1] * depth, rows.shape[3])
    picked = lax.dot_general(
        lhs, flat, (((2,), (1,)), ((0,), (0,))), preferred_element_type=jnp.float32
    )
    return picked.astype(jnp.bfloat16).reshape(rows.shape[0], pick.shape[0], depth, rows.shape[3])


def with_halo(cells, width, edge_rows=None):
    count = lax.axis_size("tiles")
    if edge_rows is None:
        edge_rows = jnp.concatenate([cells[..., :width, :], cells[..., cells.shape[-2] - width :, :]], axis=-2)
    head = edge_rows[..., :width, :]
    tail = edge_rows[..., width:, :]
    from_above = lax.ppermute(tail, "tiles", [(i, i + 1) for i in range(count - 1)])
    from_below = lax.ppermute(head, "tiles", [(i + 1, i) for i in range(count - 1)])
    return jnp.concatenate([from_above, cells, from_below], axis=-2)


def quantile_map(values, anchor, increments):
    step_x = increments[:, 0].astype(jnp.float32)
    step_y = increments[:, 1].astype(jnp.float32)
    ends = anchor[:, 0][:, None, :].astype(jnp.float32) + jnp.cumsum(step_x, axis=1)
    position = jnp.concatenate([anchor[:, 0][:, None, :].astype(jnp.float32), ends], axis=1)
    slopes = step_y / step_x
    zero = jnp.zeros_like(slopes[:, :1])
    bends = jnp.concatenate([slopes, zero], axis=1) - jnp.concatenate([zero, slopes], axis=1)
    offset = anchor[:, 1].astype(jnp.float32) - jnp.sum(bends * position, axis=1)
    above = jnp.maximum(values.astype(jnp.float32)[:, :, None, :], position[:, None])
    total = jnp.sum(bends[:, None] * above, axis=2)
    return (offset[:, None, :] + total).astype(jnp.bfloat16)


def body(observed, knot_base, knot_steps, block_route, land_mask, terrain):
    day_count, row_count, columns = observed.shape
    ntiles = lax.axis_size("tiles")
    ndays = lax.axis_size("days")
    owned = row_count // 2
    quarter = knot_base.shape[2]
    served = block_route.shape[0]
    tile_ids = jnp.arange(ntiles, dtype=jnp.int32)

    target = block_route // owned
    place_slot = block_route % owned
    match = target[None, :] == tile_ids[:, None]
    has = jnp.any(match, axis=1)
    slot_table = jnp.where(has, jnp.sum(jnp.where(match, place_slot[None, :], 0), axis=1), owned)

    lanes = 128
    recv_rows = lax.all_to_all(
        jnp.broadcast_to(slot_table.astype(jnp.int32)[:, None], (ntiles, lanes)),
        "tiles", 0, 0, tiled=True,
    )

    slot_ids = jnp.arange(owned, dtype=jnp.int32)
    holder = jnp.sum(
        jnp.where(recv_rows[:, :owned] == slot_ids[None, :], tile_ids[:, None], 0), axis=0
    )

    pair = ("days", "tiles")
    send_pick = (recv_rows[:, :owned] == slot_ids[None, :]).astype(jnp.bfloat16)
    local = observed.reshape(day_count, owned, ndays, quarter).transpose(2, 1, 0, 3)
    outgoing = select_rows(send_pick, local).reshape(ndays * ntiles, day_count, quarter)
    arrived = lax.all_to_all(outgoing, pair, 0, 0, tiled=True)
    arrived = arrived.reshape(ndays, ntiles, day_count, quarter)
    own_rows = jnp.take(arrived, target, axis=1, mode="clip").transpose(1, 0, 2, 3)
    own_rows = own_rows.reshape(served, ndays * day_count, quarter)

    mapped_part = quantile_map(own_rows, knot_base, knot_steps)

    mapped_part = mapped_part.reshape(served, ndays, day_count, quarter).transpose(1, 0, 2, 3)
    packed = select_rows(match.astype(jnp.bfloat16), mapped_part)
    packed = packed.reshape(ndays * ntiles, day_count, quarter)
    returned = lax.all_to_all(packed, pair, 0, 0, tiled=True)
    returned = returned.reshape(ndays, ntiles, day_count, quarter)
    blocks = jnp.take(returned, holder, axis=1, mode="clip")
    mapped = blocks.transpose(2, 1, 0, 3).reshape(day_count, row_count, columns)
    edge_count = PASSES // 2
    edges = jnp.concatenate([holder[:edge_count], holder[owned - edge_count :]])
    edge_rows = jnp.take(returned, edges, axis=1, mode="clip").transpose(2, 1, 0, 3)
    edge_rows = edge_rows.reshape(day_count, 2 * PASSES, columns)

    depth = PASSES
    weights = terrain * land_mask.astype(jnp.float32)
    wide_maps = with_halo(jnp.stack([weights, terrain]), depth)
    wide_weights = wide_maps[0]
    wide_center = center_share * wide_maps[1]
    wide_denom = wide_center + neighbour_sum(jnp.pad(wide_weights, 1))
    wide_denom = jnp.where(wide_denom > 0.0, wide_denom, 1.0)
    own_weights = wide_weights[depth : depth + row_count]
    own_center = wide_center[depth : depth + row_count]
    own_denom = wide_denom[depth : depth + row_count]
    field = mapped.astype(jnp.float32)
    inner = smoothed(field, own_weights, own_center, own_denom)
    wide_field = with_halo(mapped, depth, edge_rows).astype(jnp.float32)
    strip = 3 * depth
    top = smoothed(
        wide_field[:, :strip], wide_weights[:strip], wide_center[:strip], wide_denom[:strip]
    )
    low = row_count + 2 * depth - strip
    bottom = smoothed(
        wide_field[:, low:], wide_weights[low:], wide_center[low:], wide_denom[low:]
    )
    return jnp.concatenate(
        [top[:, depth : 2 * depth], inner[:, depth : row_count - depth], bottom[:, depth : 2 * depth]],
        axis=1,
    )


def solution(mesh):
    return jax.shard_map(
        body,
        mesh=mesh,
        in_specs=(
            P("days", "tiles", None),
            P("tiles", None, "days"),
            P("tiles", None, None, "days"),
            P("tiles"),
            P("tiles", None),
            P("tiles", None),
        ),
        out_specs=P("days", "tiles", None),
        check_vma=False,
    )
```

```python
import jax
import jax.numpy as jnp
from jax import lax
from jax.sharding import PartitionSpec as P

PASSES = 4


center_share = 0.5


def neighbour_sum(padded):
    return (
        padded[..., :-2, 1:-1]
        + padded[..., 2:, 1:-1]
        + padded[..., 1:-1, :-2]
        + padded[..., 1:-1, 2:]
    )


def smoothed(field, weights, center, denom):
    for sweep in range(PASSES):
        padded = jnp.pad(field * weights[None], ((0, 0), (1, 1), (1, 1)))
        field = (center[None] * field + neighbour_sum(padded)) / denom[None]
    return field


def with_halo(cells, width, edge_rows=None):
    count = lax.axis_size("tiles")
    if edge_rows is None:
        edge_rows = jnp.concatenate([cells[..., :width, :], cells[..., cells.shape[-2] - width :, :]], axis=-2)
    head = edge_rows[..., :width, :]
    tail = edge_rows[..., width:, :]
    from_above = lax.ppermute(tail, "tiles", [(i, i + 1) for i in range(count - 1)])
    from_below = lax.ppermute(head, "tiles", [(i + 1, i) for i in range(count - 1)])
    return jnp.concatenate([from_above, cells, from_below], axis=-2)


def quantile_map(values, anchor, increments):
    step_x = increments[:, 0].astype(jnp.float32)
    step_y = increments[:, 1].astype(jnp.float32)
    ends = anchor[:, 0][:, None, :].astype(jnp.float32) + jnp.cumsum(step_x, axis=1)
    position = jnp.concatenate([anchor[:, 0][:, None, :].astype(jnp.float32), ends], axis=1)
    slopes = step_y / step_x
    zero = jnp.zeros_like(slopes[:, :1])
    bends = jnp.concatenate([slopes, zero], axis=1) - jnp.concatenate([zero, slopes], axis=1)
    offset = anchor[:, 1].astype(jnp.float32) - jnp.sum(bends * position, axis=1)
    above = jnp.maximum(values.astype(jnp.float32)[:, :, None, :], position[:, None])
    total = jnp.sum(bends[:, None] * above, axis=2)
    return (offset[:, None, :] + total).astype(jnp.bfloat16)


def body(observed, knot_base, knot_steps, block_route, land_mask, terrain):
    day_count, row_count, columns = observed.shape
    ntiles = lax.axis_size("tiles")
    ndays = lax.axis_size("days")
    owned = row_count // 2
    quarter = knot_base.shape[2]
    served = block_route.shape[0]
    tile_ids = jnp.arange(ntiles, dtype=jnp.int32)

    target = block_route // owned
    place_slot = block_route % owned
    match = target[None, :] == tile_ids[:, None]
    has = jnp.any(match, axis=1)
    slot_table = jnp.where(has, jnp.sum(jnp.where(match, place_slot[None, :], 0), axis=1), owned)
    local_of = jnp.sum(jnp.where(match, jnp.arange(served, dtype=jnp.int32)[None, :], 0), axis=1)

    lanes = 128
    lane_slots = jnp.broadcast_to(place_slot[None, :, None], (ntiles, served, lanes))
    send_rows = jnp.sum(jnp.where(match[:, :, None], lane_slots + 1, 0), axis=1) - 1
    send_rows = jnp.where(send_rows < 0, owned, send_rows)
    recv_rows = lax.all_to_all(send_rows.astype(jnp.int32), "tiles", 0, 0, tiled=True)

    picked = jnp.minimum(recv_rows[:, 0], owned - 1)
    slot_ids = jnp.arange(owned, dtype=jnp.int32)
    holder = jnp.sum(
        jnp.where(recv_rows[:, :owned] == slot_ids[None, :], tile_ids[:, None], 0), axis=0
    )

    local = observed.reshape(day_count, owned, ndays, quarter)
    outgoing = jnp.take(local, picked, axis=1, mode="clip")
    outgoing = outgoing.transpose(1, 2, 0, 3).reshape(ntiles * ndays, day_count, quarter)
    arrived = lax.all_to_all(outgoing, ("tiles", "days"), 0, 0, tiled=True)
    arrived = arrived.reshape(ntiles, ndays * day_count, quarter)
    own_rows = jnp.take(arrived, target, axis=0, mode="clip")

    mapped_part = quantile_map(own_rows, knot_base, knot_steps)

    packed = jnp.take(mapped_part, local_of, axis=0, mode="clip")
    packed = packed.reshape(ntiles * ndays, day_count, quarter)
    returned = lax.all_to_all(packed, ("tiles", "days"), 0, 0, tiled=True)
    returned = returned.reshape(ntiles, ndays, day_count, quarter)
    blocks = jnp.take(returned, holder, axis=0, mode="clip")
    mapped = blocks.transpose(2, 0, 1, 3).reshape(day_count, row_count, columns)
    edge_count = PASSES // 2
    edges = jnp.concatenate([holder[:edge_count], holder[owned - edge_count :]])
    edge_rows = jnp.take(returned, edges, axis=0, mode="clip").transpose(2, 0, 1, 3)
    edge_rows = edge_rows.reshape(day_count, 2 * PASSES, columns)

    depth = PASSES
    weights = terrain * land_mask.astype(jnp.float32)
    wide_maps = with_halo(jnp.stack([weights, terrain]), depth)
    wide_weights = wide_maps[0]
    wide_center = center_share * wide_maps[1]
    wide_denom = wide_center + neighbour_sum(jnp.pad(wide_weights, 1))
    wide_denom = jnp.where(wide_denom > 0.0, wide_denom, 1.0)
    own_weights = wide_weights[depth : depth + row_count]
    own_center = wide_center[depth : depth + row_count]
    own_denom = wide_denom[depth : depth + row_count]
    field = mapped.astype(jnp.float32)
    inner = smoothed(field, own_weights, own_center, own_denom)
    wide_field = with_halo(mapped, depth, edge_rows).astype(jnp.float32)
    strip = 3 * depth
    top = smoothed(
        wide_field[:, :strip], wide_weights[:strip], wide_center[:strip], wide_denom[:strip]
    )
    low = row_count + 2 * depth - strip
    bottom = smoothed(
        wide_field[:, low:], wide_weights[low:], wide_center[low:], wide_denom[low:]
    )
    return jnp.concatenate(
        [top[:, depth : 2 * depth], inner[:, depth : row_count - depth], bottom[:, depth : 2 * depth]],
        axis=1,
    )


def solution(mesh):
    return jax.shard_map(
        body,
        mesh=mesh,
        in_specs=(
            P("days", "tiles", None),
            P("tiles", None, "days"),
            P("tiles", None, None, "days"),
            P("tiles"),
            P("tiles", None),
            P("tiles", None),
        ),
        out_specs=P("days", "tiles", None),
        check_vma=False,
    )
```

```python
import jax
import jax.numpy as jnp
from jax import lax
from jax.sharding import PartitionSpec as P

PASSES = 4


center_share = 0.5


def neighbour_sum(padded):
    return (
        padded[..., :-2, 1:-1]
        + padded[..., 2:, 1:-1]
        + padded[..., 1:-1, :-2]
        + padded[..., 1:-1, 2:]
    )


def smoothed(field, weights, center, denom):
    edges = [(0, 0)] * (field.ndim - 2) + [(1, 1), (1, 1)]
    for sweep in range(PASSES):
        padded = jnp.pad(field * weights, edges)
        field = (center * field + neighbour_sum(padded)) / denom
    return field


def with_halo(cells, width, edge_rows=None):
    count = lax.axis_size("tiles")
    if edge_rows is None:
        edge_rows = jnp.concatenate([cells[..., :width, :], cells[..., cells.shape[-2] - width :, :]], axis=-2)
    head = edge_rows[..., :width, :]
    tail = edge_rows[..., width:, :]
    from_above = lax.ppermute(tail, "tiles", [(i, i + 1) for i in range(count - 1)])
    from_below = lax.ppermute(head, "tiles", [(i + 1, i) for i in range(count - 1)])
    return jnp.concatenate([from_above, cells, from_below], axis=-2)


def quantile_map(values, anchor, increments):
    step_x = increments[:, 0].astype(jnp.float32)
    step_y = increments[:, 1].astype(jnp.float32)
    ends = anchor[:, 0][:, None, :].astype(jnp.float32) + jnp.cumsum(step_x, axis=1)
    position = jnp.concatenate([anchor[:, 0][:, None, :].astype(jnp.float32), ends], axis=1)
    slopes = step_y / step_x
    zero = jnp.zeros_like(slopes[:, :1])
    bends = jnp.concatenate([slopes, zero], axis=1) - jnp.concatenate([zero, slopes], axis=1)
    offset = anchor[:, 1].astype(jnp.float32) - jnp.sum(bends * position, axis=1)
    above = jnp.maximum(values.astype(jnp.float32)[:, :, None, :], position[:, None])
    total = jnp.sum(bends[:, None] * above, axis=2)
    return (offset[:, None, :] + total).astype(jnp.bfloat16)


def body(observed, knot_base, knot_steps, block_route, land_mask, terrain):
    day_count, row_count, columns = observed.shape
    ntiles = lax.axis_size("tiles")
    ndays = lax.axis_size("days")
    owned = row_count // 2
    quarter = knot_base.shape[2]
    served = block_route.shape[0]
    tile_ids = jnp.arange(ntiles, dtype=jnp.int32)

    target = block_route // owned
    place_slot = block_route % owned
    match = target[None, :] == tile_ids[:, None]
    has = jnp.any(match, axis=1)
    slot_table = jnp.where(has, jnp.sum(jnp.where(match, place_slot[None, :], 0), axis=1), owned)
    local_of = jnp.sum(jnp.where(match, jnp.arange(served, dtype=jnp.int32)[None, :], 0), axis=1)

    lanes = 128
    recv_rows = lax.all_to_all(
        jnp.broadcast_to(slot_table.astype(jnp.int32)[:, None], (ntiles, lanes)),
        "tiles", 0, 0, tiled=True,
    )

    picked = jnp.minimum(recv_rows[:, 0], owned - 1)
    slot_ids = jnp.arange(owned, dtype=jnp.int32)
    holder = jnp.sum(
        jnp.where(recv_rows[:, :owned] == slot_ids[None, :], tile_ids[:, None], 0), axis=0
    )

    local = observed.reshape(day_count, owned, ndays, quarter)
    outgoing = jnp.take(local, picked, axis=1, mode="clip")
    outgoing = outgoing.transpose(1, 2, 0, 3).reshape(ntiles * ndays, day_count, quarter)
    arrived = lax.all_to_all(outgoing, ("tiles", "days"), 0, 0, tiled=True)
    arrived = arrived.reshape(ntiles, ndays * day_count, quarter)
    own_rows = jnp.take(arrived, target, axis=0, mode="clip")

    mapped_part = quantile_map(own_rows, knot_base, knot_steps)

    packed = jnp.take(mapped_part, local_of, axis=0, mode="clip")
    packed = packed.reshape(ntiles * ndays, day_count, quarter)
    returned = lax.all_to_all(packed, ("tiles", "days"), 0, 0, tiled=True)
    returned = returned.reshape(ntiles, ndays, day_count, quarter)
    blocks = jnp.take(returned, holder, axis=0, mode="clip")
    mapped = blocks.transpose(2, 0, 1, 3).reshape(day_count, row_count, columns)
    edge_count = PASSES // 2
    edges = jnp.concatenate([holder[:edge_count], holder[owned - edge_count :]])
    edge_rows = jnp.take(returned, edges, axis=0, mode="clip").transpose(2, 0, 1, 3)
    edge_rows = edge_rows.reshape(day_count, 2 * PASSES, columns)

    depth = PASSES
    weights = terrain * land_mask.astype(jnp.float32)
    wide_maps = with_halo(jnp.stack([weights, terrain]), depth)
    wide_weights = wide_maps[0]
    wide_center = center_share * wide_maps[1]
    wide_denom = wide_center + neighbour_sum(jnp.pad(wide_weights, 1))
    wide_denom = jnp.where(wide_denom > 0.0, wide_denom, 1.0)
    own_weights = wide_weights[depth : depth + row_count]
    own_center = wide_center[depth : depth + row_count]
    own_denom = wide_denom[depth : depth + row_count]
    field = mapped.astype(jnp.float32)
    inner = smoothed(field, own_weights[None], own_center[None], own_denom[None])
    wide_field = with_halo(mapped, depth, edge_rows).astype(jnp.float32)
    strip = 3 * depth
    low = row_count + 2 * depth - strip
    def ends(rows):
        return jnp.stack([rows[..., :strip, :], rows[..., low:, :]])
    strips = smoothed(
        ends(wide_field), ends(wide_weights)[:, None], ends(wide_center)[:, None], ends(wide_denom)[:, None]
    )
    return jnp.concatenate(
        [strips[0][:, depth : 2 * depth], inner[:, depth : row_count - depth], strips[1][:, depth : 2 * depth]],
        axis=1,
    )


def solution(mesh):
    return jax.shard_map(
        body,
        mesh=mesh,
        in_specs=(
            P("days", "tiles", None),
            P("tiles", None, "days"),
            P("tiles", None, None, "days"),
            P("tiles"),
            P("tiles", None),
            P("tiles", None),
        ),
        out_specs=P("days", "tiles", None),
        check_vma=False,
    )
```
